1024 devices in a mesh: az: 16 (over x, core), rad: 8 (over y), vert: 8 (over z).
Axes of the slice: x: 8, y: 8, z: 8, core: 2. Of those that a mesh axis runs over, the one named last changes fastest.
Arguments:
- fields: float32 [8, 128, 64, 2048], P(None, 'rad', 'vert', 'az'), may hold values from -6 to 6
- shear_shift: int32 [128], P('rad'), may hold values from 0 to 2047, as said below
- remap_fraction: float32 [128], P('rad'), may hold values from 0 to 1
- diffusivity: float32 [8], replicated, may hold values from 0.03 to 0.12
Outputs:
- advected: float32 [8, 128, 64, 2048], P(None, 'rad', 'vert', 'az')
The draws below stay inside these ranges and needn't reach their ends.
Inputs may be any that keep to these rules, and one draw needn't show every extreme that they name: `shear_shift`: each radial row's integer shift; some row has 0 and some row has 2047.
All inputs are finite; a program needn't handle non-finite values.
Results may differ from the reference program's by a relative error of at most 0.00002.
Values sent between devices are 32-bit elements; how exact they have to be, the bound alone decides.
No kernel may reach another device: no remote copies, remote signals or barrier semaphores. Data moves between devices by JAX's collectives and lax.ppermute only.
A program may use at most 32 MiB of HBM per device.

```python
import math
import jax
import jax.numpy as jnp
from jax import lax

FIELDS = 8
NR = 128
NZ = 64
NA = 2048


def draw_shear_shift(key, part):
    key_values = jax.random.fold_in(key, 11)
    key_first = jax.random.fold_in(key, 12)
    key_second = jax.random.fold_in(key, 13)
    values = jax.random.randint(key_values, (NR,), 0, NA, dtype=jnp.int32)
    first_row = jax.random.randint(key_first, (), 0, NR, dtype=jnp.int32)
    offset_row = jax.random.randint(key_second, (), 1, NR, dtype=jnp.int32)
    second_row = (first_row + offset_row) % NR
    values = values.at[first_row].set(NA - 1)
    values = values.at[second_row].set(0)
    return values


def block_levels(own_key, dims, cuts, low, largest):
    gain = 1.0
    for position, shards_of in cuts:
        steps = jax.random.uniform(jax.random.fold_in(jax.random.fold_in(own_key, 6), position), (shards_of,), jnp.float32, low / len(cuts), largest / len(cuts))
        gain = gain * jnp.repeat(jnp.exp(steps), dims[position] // shards_of).reshape((-1,) + (1,) * (len(dims) - 1 - position))
    return gain


def bell_draw(own_key, shape, scale, bound, pieces=(), held_as=jnp.bfloat16):
    result = jax.random.normal(own_key, shape, jnp.float32) * scale
    if len(pieces) > 0:
        result = block_levels(own_key, shape, pieces, -0.22, 0.18) * result
    return jnp.clip(result, min=-bound, max=bound).astype(held_as)


def setup_inputs(seed: int = 0) -> dict:
    keys = jax.random.split(jax.random.key(seed), 5)
    fields = bell_draw(keys[0], (FIELDS, NR, NZ, NA), 1.0, 6.0, ((1, 8), (2, 8), (3, 16)), jnp.float32)
    shear_shift = draw_shear_shift(jax.random.fold_in(keys[4], 71), 0)
    remap_fraction = jnp.clip(1.0 * jax.random.uniform(keys[2], (NR,), jnp.float32) ** block_levels(keys[2], (NR,), ((0, 8),), -0.2, 0.2), 0.0, 1.0)
    diffusivity = jnp.clip(jnp.exp(jax.random.uniform(keys[3], (FIELDS,), jnp.float32, math.log(0.03), math.log(0.12))), 0.03, 0.12)
    return {"fields": fields, "shear_shift": shear_shift, "remap_fraction": remap_fraction, "diffusivity": diffusivity}


def reference(fields, shear_shift, remap_fraction, diffusivity):
    columns = jnp.arange(NA, dtype=jnp.int32)
    source = ((columns[None, :] - shear_shift[:, None]) % NA).astype(jnp.int32)
    fraction = remap_fraction[:, None, None]

    def per_field(pair):
        field, coefficient = pair
        shifted = jnp.take_along_axis(field, jnp.broadcast_to(source[:, None, :], field.shape), axis=2)
        padded = jnp.pad(shifted, ((1, 1), (1, 1), (0, 0)))
        laplace = padded[2:, 1:-1] + padded[:-2, 1:-1] + padded[1:-1, 2:] + padded[1:-1, :-2] - 4.0 * shifted
        diffused = shifted + coefficient * laplace
        after = jnp.roll(diffused, -1, axis=2)
        before = jnp.roll(diffused, 1, axis=2)
        return diffused - 0.5 * fraction * (after - before) + 0.5 * fraction * fraction * (after - 2.0 * diffused + before)

    return lax.map(per_field, (fields, diffusivity))
```

```python
import jax
import jax.numpy as jnp
from jax import lax
from jax.sharding import PartitionSpec as P


def barrel(block, amounts, span):
    result = block
    for level in range(span.bit_length()):
        moved = jnp.roll(result, 1 << level, axis=2)
        chosen = amounts // (1 << level) % 2 == 1
        result = jnp.where(chosen[:, None, None], moved, result)
    return result


def halo_pairs(rows, halves, fields, step):
    pairs = []
    for r in range(rows):
        for f in range(fields):
            for h in range(halves):
                nh, nr = h + step, r
                if nh == halves:
                    nh, nr = 0, r + 1
                elif nh < 0:
                    nh, nr = halves - 1, r - 1
                if 0 <= nr < rows:
                    pairs.append(((f * halves + h) * rows + r, (f * halves + nh) * rows + nr))
    return pairs


def per_device(fields, shear_shift, remap_fraction, diffusivity):
    nf, nrow, nz, width = fields.shape
    loop = lax.axis_size("az")
    halves = loop // nf
    rows = nrow // halves
    x = fields.reshape(nf * halves, rows, nz, width)
    y = lax.all_to_all(x, "az", 0, 3, tiled=True)[0]
    length = y.shape[2]
    me = lax.axis_index("az")
    f = me // halves
    h = me % halves
    amounts = lax.dynamic_slice_in_dim(shear_shift, h * rows, rows)
    fraction = lax.dynamic_slice_in_dim(remap_fraction, h * rows, rows)[:, None, None]
    coefficient = diffusivity[f]
    shifted = barrel(y, amounts, length - 1)

    nrad = lax.axis_size("rad")
    nvert = lax.axis_size("vert")
    both = ("az", "rad")
    prev_row = lax.ppermute(shifted[-1:], both, halo_pairs(nrad, halves, nf, 1))
    next_row = lax.ppermute(shifted[:1], both, halo_pairs(nrad, halves, nf, -1))
    up = [(i, i + 1) for i in range(nvert - 1)]
    down = [(i + 1, i) for i in range(nvert - 1)]
    below = lax.ppermute(shifted[:, -1:], "vert", up)
    above = lax.ppermute(shifted[:, :1], "vert", down)

    r_plus = jnp.concatenate([shifted[1:], next_row], axis=0)
    r_minus = jnp.concatenate([prev_row, shifted[:-1]], axis=0)
    z_plus = jnp.concatenate([shifted[:, 1:], above], axis=1)
    z_minus = jnp.concatenate([below, shifted[:, :-1]], axis=1)
    laplace = r_plus + r_minus + z_plus + z_minus - 4.0 * shifted
    diffused = shifted + coefficient * laplace
    after = jnp.roll(diffused, -1, axis=2)
    before = jnp.roll(diffused, 1, axis=2)
    out = (
        diffused
        - 0.5 * fraction * (after - before)
        + 0.5 * fraction * fraction * (after - 2.0 * diffused + before)
    )
    back = lax.all_to_all(out[None], "az", 3, 0, tiled=True)
    return back.reshape(nf, nrow, nz, width)


def solution(mesh):
    in_specs = (P(None, "rad", "vert", "az"), P("rad"), P("rad"), P())
    out_specs = P(None, "rad", "vert", "az")
    return jax.shard_map(
        per_device, mesh=mesh, in_specs=in_specs, out_specs=out_specs, check_vma=False
    )
```

```python
import jax
import jax.numpy as jnp
from jax import lax
from jax.sharding import PartitionSpec as P


def barrel(block, amounts, span):
    result = block
    for level in range(span.bit_length()):
        moved = jnp.roll(result, 1 << level, axis=2)
        chosen = amounts // (1 << level) % 2 == 1
        result = jnp.where(chosen[:, None, None], moved, result)
    return result


def halo_pairs(rows, halves, fields, step):
    pairs = []
    for r in range(rows):
        for f in range(fields):
            for h in range(halves):
                nh, nr = h + step, r
                if nh == halves:
                    nh, nr = 0, r + 1
                elif nh < 0:
                    nh, nr = halves - 1, r - 1
                if 0 <= nr < rows:
                    pairs.append(((f * halves + h) * rows + r, (f * halves + nh) * rows + nr))
    return pairs


def per_device(fields, shear_shift, remap_fraction, diffusivity):
    nf, nrow, nz, width = fields.shape
    loop = lax.axis_size("az")
    halves = loop // nf
    rows = nrow // halves
    x = fields.reshape(nf * halves, rows, nz, width)
    y = lax.all_to_all(x, "az", 0, 0, tiled=True)
    y = jnp.transpose(y, (1, 2, 0, 3)).reshape(rows, nz, loop * width)
    length = y.shape[2]
    me = lax.axis_index("az")
    f = me // halves
    h = me % halves
    amounts = lax.dynamic_slice_in_dim(shear_shift, h * rows, rows)
    fraction = lax.dynamic_slice_in_dim(remap_fraction, h * rows, rows)[:, None, None]
    coefficient = diffusivity[f]
    shifted = barrel(y, amounts, length - 1)

    nrad = lax.axis_size("rad")
    nvert = lax.axis_size("vert")
    both = ("az", "rad")
    prev_row = lax.ppermute(shifted[-1:], both, halo_pairs(nrad, halves, nf, 1))
    next_row = lax.ppermute(shifted[:1], both, halo_pairs(nrad, halves, nf, -1))
    up = [(i, i + 1) for i in range(nvert - 1)]
    down = [(i + 1, i) for i in range(nvert - 1)]
    below = lax.ppermute(shifted[:, -1:], "vert", up)
    above = lax.ppermute(shifted[:, :1], "vert", down)

    r_plus = jnp.concatenate([shifted[1:], next_row], axis=0)
    r_minus = jnp.concatenate([prev_row, shifted[:-1]], axis=0)
    z_plus = jnp.concatenate([shifted[:, 1:], above], axis=1)
    z_minus = jnp.concatenate([below, shifted[:, :-1]], axis=1)
    laplace = r_plus + r_minus + z_plus + z_minus - 4.0 * shifted
    diffused = shifted + coefficient * laplace
    after = jnp.roll(diffused, -1, axis=2)
    before = jnp.roll(diffused, 1, axis=2)
    out = (
        diffused
        - 0.5 * fraction * (after - before)
        + 0.5 * fraction * fraction * (after - 2.0 * diffused + before)
    )
    blocks = jnp.transpose(out.reshape(rows, nz, loop, width), (2, 0, 1, 3))
    back = lax.all_to_all(blocks, "az", 0, 0, tiled=True)
    return back.reshape(nf, nrow, nz, width)


def solution(mesh):
    in_specs = (P(None, "rad", "vert", "az"), P("rad"), P("rad"), P())
    out_specs = P(None, "rad", "vert", "az")
    return jax.shard_map(
        per_device, mesh=mesh, in_specs=in_specs, out_specs=out_specs, check_vma=False
    )
```

```python
import jax
import jax.numpy as jnp
from jax import lax
from jax.experimental import pallas as pl
from jax.experimental.pallas import tpu as pltpu
from jax.sharding import PartitionSpec as P


def shift_kernel(amount_ref, x_ref, o_ref, last_ref, first_ref, low_ref, high_ref):
    nblk, rows, nz, width = x_ref.shape
    lane = lax.broadcasted_iota(jnp.int32, (nz, width), 1)
    for k in range(rows):
        s = amount_ref[k]
        b = s // width
        rem = s % width
        late = lane >= width - rem
        for j in range(nblk):
            near = x_ref[(j - b + nblk) % nblk, k]
            far = x_ref[(j - b - 1 + 2 * nblk) % nblk, k]
            v = pltpu.roll(jnp.where(late, far, near), rem, 1)
            cols = slice(j * width, (j + 1) * width)
            o_ref[k, :, cols] = v
            low_ref[k : k + 1, cols] = v[0:1]
            high_ref[k : k + 1, cols] = v[nz - 1 : nz]
            if k == 0:
                first_ref[0, :, cols] = v
            if k == rows - 1:
                last_ref[0, :, cols] = v


def diffuse_kernel(c_ref, e_ref, s_ref, prev_ref, next_ref, below_ref, above_ref, o_ref):
    nblk, rows, nz, width = o_ref.shape
    length = s_ref.shape[2]
    sub = lax.broadcasted_iota(jnp.int32, (nz, length), 0)
    c = c_ref[0]
    for k in range(rows):
        shifted = s_ref[k]
        r_plus = s_ref[k + 1] if k < rows - 1 else next_ref[0]
        r_minus = s_ref[k - 1] if k > 0 else prev_ref[0]
        z_plus = jnp.where(sub == nz - 1, above_ref[k : k + 1, :], pltpu.roll(shifted, nz - 1, 0))
        z_minus = jnp.where(sub == 0, below_ref[k : k + 1, :], pltpu.roll(shifted, 1, 0))
        laplace = r_plus + r_minus + z_plus + z_minus - 4.0 * shifted
        diffused = shifted + c * laplace
        after = pltpu.roll(diffused, length - 1, 1)
        before = pltpu.roll(diffused, 1, 1)
        e = e_ref[k]
        half = 0.5 * e
        out = diffused - half * (after - before) + half * e * (after - 2.0 * diffused + before)
        for j in range(nblk):
            o_ref[j, k] = out[:, j * width : (j + 1) * width]


def barrel(block, amounts, span):
    result = block
    for level in range(span.bit_length()):
        moved = jnp.roll(result, 1 << level, axis=2)
        chosen = amounts // (1 << level) % 2 == 1
        result = jnp.where(chosen[:, None, None], moved, result)
    return result


def halo_pairs(rows, halves, fields, step):
    pairs = []
    for r in range(rows):
        for f in range(fields):
            for h in range(halves):
                nh, nr = h + step, r
                if nh == halves:
                    nh, nr = 0, r + 1
                elif nh < 0:
                    nh, nr = halves - 1, r - 1
                if 0 <= nr < rows:
                    pairs.append(((f * halves + h) * rows + r, (f * halves + nh) * rows + nr))
    return pairs


def per_device(fields, shear_shift, remap_fraction, diffusivity):
    nf, nrow, nz, width = fields.shape
    loop = lax.axis_size("az")
    halves = loop // nf
    rows = nrow // halves
    x = fields.reshape(nf * halves, rows, nz, width)
    y = lax.all_to_all(x, "az", 0, 0, tiled=True)
    me = lax.axis_index("az")
    f = me // halves
    h = me % halves
    amounts = lax.dynamic_slice_in_dim(shear_shift, h * rows, rows)
    fraction = lax.dynamic_slice_in_dim(remap_fraction, h * rows, rows)
    coefficient = lax.dynamic_slice_in_dim(diffusivity, f, 1)
    length = loop * width
    smem = pl.BlockSpec(memory_space=pltpu.SMEM)
    vmem = pl.BlockSpec(memory_space=pltpu.VMEM)
    shifted, last, first, low, high = pl.pallas_call(
        shift_kernel,
        out_shape=(
            jax.ShapeDtypeStruct((rows, nz, length), y.dtype),
            jax.ShapeDtypeStruct((1, nz, length), y.dtype),
            jax.ShapeDtypeStruct((1, nz, length), y.dtype),
            jax.ShapeDtypeStruct((rows, length), y.dtype),
            jax.ShapeDtypeStruct((rows, length), y.dtype),
        ),
        in_specs=[smem, vmem],
        out_specs=(vmem,) * 5,
    )(amounts, y)

    nrad = lax.axis_size("rad")
    nvert = lax.axis_size("vert")
    both = ("az", "rad")
    prev_row = lax.ppermute(last, both, halo_pairs(nrad, halves, nf, 1))
    next_row = lax.ppermute(first, both, halo_pairs(nrad, halves, nf, -1))
    up = [(i, i + 1) for i in range(nvert - 1)]
    down = [(i + 1, i) for i in range(nvert - 1)]
    below = lax.ppermute(high, "vert", up)
    above = lax.ppermute(low, "vert", down)

    blocks = pl.pallas_call(
        diffuse_kernel,
        out_shape=jax.ShapeDtypeStruct((loop, rows, nz, width), y.dtype),
        in_specs=[smem, smem] + [vmem] * 5,
        out_specs=vmem,
    )(coefficient, fraction, shifted, prev_row, next_row, below, above)
    back = lax.all_to_all(blocks, "az", 0, 0, tiled=True)
    return back.reshape(nf, nrow, nz, width)


def solution(mesh):
    in_specs = (P(None, "rad", "vert", "az"), P("rad"), P("rad"), P())
    out_specs = P(None, "rad", "vert", "az")
    return jax.shard_map(
        per_device, mesh=mesh, in_specs=in_specs, out_specs=out_specs, check_vma=False
    )
```

```python
import functools

import jax
import jax.numpy as jnp
from jax import lax
from jax.experimental import pallas as pl
from jax.experimental.pallas import tpu as pltpu
from jax.sharding import PartitionSpec as P

ROUNDS = 2


def shift_kernel(parts, amount_ref, x_ref, o_ref, last_ref, first_ref, low_ref, high_ref):
    nblk, rows, nz, width = x_ref.shape
    lane = lax.broadcasted_iota(jnp.int32, (nz, width), 1)
    base = lax.axis_index("az") % parts * rows
    for k in range(rows):
        s = amount_ref[base + k]
        b = s // width
        rem = s % width
        late = lane >= width - rem
        for j in range(nblk):
            near = x_ref[(j - b + nblk) % nblk, k]
            far = x_ref[(j - b - 1 + 2 * nblk) % nblk, k]
            v = pltpu.roll(jnp.where(late, far, near), rem, 1)
            cols = slice(j * width, (j + 1) * width)
            o_ref[k, :, cols] = v
            low_ref[k : k + 1, cols] = v[0:1]
            high_ref[k : k + 1, cols] = v[nz - 1 : nz]
            if k == 0:
                first_ref[0, :, cols] = v
            if k == rows - 1:
                last_ref[0, :, cols] = v


def diffuse_kernel(parts, offset, c_ref, e_ref, s_ref, prev_ref, next_ref, below_ref, above_ref, o_ref):
    nblk, rows, nz, width = o_ref.shape
    length = s_ref.shape[2]
    sub = lax.broadcasted_iota(jnp.int32, (nz, length), 0)
    me = lax.axis_index("az")
    base = me % parts * rows
    c = c_ref[me // parts + offset]
    for k in range(rows):
        shifted = s_ref[k]
        r_plus = s_ref[k + 1] if k < rows - 1 else next_ref[0]
        r_minus = s_ref[k - 1] if k > 0 else prev_ref[0]
        z_plus = jnp.where(sub == nz - 1, above_ref[k : k + 1, :], pltpu.roll(shifted, nz - 1, 0))
        z_minus = jnp.where(sub == 0, below_ref[k : k + 1, :], pltpu.roll(shifted, 1, 0))
        laplace = r_plus + r_minus + z_plus + z_minus - 4.0 * shifted
        diffused = shifted + c * laplace
        after = pltpu.roll(diffused, length - 1, 1)
        before = pltpu.roll(diffused, 1, 1)
        e = e_ref[base + k]
        half = 0.5 * e
        out = diffused - half * (after - before) + half * e * (after - 2.0 * diffused + before)
        for j in range(nblk):
            o_ref[j, k] = out[:, j * width : (j + 1) * width]


def halo_pairs(rows, halves, fields, step):
    pairs = []
    for r in range(rows):
        for f in range(fields):
            for h in range(halves):
                nh, nr = h + step, r
                if nh == halves:
                    nh, nr = 0, r + 1
                elif nh < 0:
                    nh, nr = halves - 1, r - 1
                if 0 <= nr < rows:
                    pairs.append(((f * halves + h) * rows + r, (f * halves + nh) * rows + nr))
    return pairs


def one_round(block, offset, shear_shift, remap_fraction, diffusivity):
    nf, nrow, nz, width = block.shape
    loop = lax.axis_size("az")
    parts = loop // nf
    rows = nrow // parts
    x = block.reshape(nf * parts, rows, nz, width)
    y = lax.all_to_all(x, "az", 0, 0, tiled=True)
    length = loop * width
    smem = pl.BlockSpec(memory_space=pltpu.SMEM)
    vmem = pl.BlockSpec(memory_space=pltpu.VMEM)
    shifted, last, first, low, high = pl.pallas_call(
        functools.partial(shift_kernel, parts),
        out_shape=(
            jax.ShapeDtypeStruct((rows, nz, length), y.dtype),
            jax.ShapeDtypeStruct((1, nz, length), y.dtype),
            jax.ShapeDtypeStruct((1, nz, length), y.dtype),
            jax.ShapeDtypeStruct((rows, length), y.dtype),
            jax.ShapeDtypeStruct((rows, length), y.dtype),
        ),
        in_specs=[smem, vmem],
        out_specs=(vmem,) * 5,
    )(shear_shift, y)

    nrad = lax.axis_size("rad")
    nvert = lax.axis_size("vert")
    both = ("az", "rad")
    prev_row = lax.ppermute(last, both, halo_pairs(nrad, parts, nf, 1))
    next_row = lax.ppermute(first, both, halo_pairs(nrad, parts, nf, -1))
    up = [(i, i + 1) for i in range(nvert - 1)]
    down = [(i + 1, i) for i in range(nvert - 1)]
    below = lax.ppermute(high, "vert", up)
    above = lax.ppermute(low, "vert", down)

    blocks = pl.pallas_call(
        functools.partial(diffuse_kernel, parts, offset),
        out_shape=jax.ShapeDtypeStruct((loop, rows, nz, width), y.dtype),
        in_specs=[smem, smem] + [vmem] * 5,
        out_specs=vmem,
    )(diffusivity, remap_fraction, shifted, prev_row, next_row, below, above)
    back = lax.all_to_all(blocks, "az", 0, 0, tiled=True)
    return back.reshape(nf, nrow, nz, width)


def per_device(fields, shear_shift, remap_fraction, diffusivity):
    nf = fields.shape[0]
    step = nf // ROUNDS
    outs = [
        one_round(fields[i : i + step], i, shear_shift, remap_fraction, diffusivity)
        for i in range(0, nf, step)
    ]
    return outs[0] if len(outs) == 1 else jnp.concatenate(outs, axis=0)


def solution(mesh):
    in_specs = (P(None, "rad", "vert", "az"), P("rad"), P("rad"), P())
    out_specs = P(None, "rad", "vert", "az")
    return jax.shard_map(
        per_device, mesh=mesh, in_specs=in_specs, out_specs=out_specs, check_vma=False
    )
```

```python
import functools

import jax
import jax.numpy as jnp
from jax import lax
from jax.experimental import pallas as pl
from jax.experimental.pallas import tpu as pltpu
from jax.sharding import PartitionSpec as P

ROUNDS = 1


def shift_kernel(parts, amount_ref, x_ref, o_ref, last_ref, first_ref, low_ref, high_ref):
    nblk, rows, nz, width = x_ref.shape
    lane = lax.broadcasted_iota(jnp.int32, (nz, width), 1)
    base = lax.axis_index("az") % parts * rows
    for k in range(rows):
        s = amount_ref[base + k]
        b = s // width
        rem = s % width
        late = lane >= width - rem
        for j in range(nblk):
            near = x_ref[(j - b + nblk) % nblk, k]
            far = x_ref[(j - b - 1 + 2 * nblk) % nblk, k]
            v = pltpu.roll(jnp.where(late, far, near), rem, 1)
            cols = slice(j * width, (j + 1) * width)
            o_ref[k, :, cols] = v
            low_ref[k : k + 1, cols] = v[0:1]
            high_ref[k : k + 1, cols] = v[nz - 1 : nz]
            if k == 0:
                first_ref[0, :, cols] = v
            if k == rows - 1:
                last_ref[0, :, cols] = v


def diffuse_kernel(parts, offset, c_ref, e_ref, s_ref, prev_ref, next_ref, below_ref, above_ref, o_ref):
    nblk, rows, nz, width = o_ref.shape
    length = s_ref.shape[2]
    sub = lax.broadcasted_iota(jnp.int32, (nz, length), 0)
    me = lax.axis_index("az")
    base = me % parts * rows
    c = c_ref[me // parts + offset]
    for k in range(rows):
        shifted = s_ref[k]
        r_plus = s_ref[k + 1] if k < rows - 1 else next_ref[0]
        r_minus = s_ref[k - 1] if k > 0 else prev_ref[0]
        z_plus = jnp.where(sub == nz - 1, above_ref[k : k + 1, :], pltpu.roll(shifted, nz - 1, 0))
        z_minus = jnp.where(sub == 0, below_ref[k : k + 1, :], pltpu.roll(shifted, 1, 0))
        laplace = r_plus + r_minus + z_plus + z_minus - 4.0 * shifted
        diffused = shifted + c * laplace
        after = pltpu.roll(diffused, length - 1, 1)
        before = pltpu.roll(diffused, 1, 1)
        e = e_ref[base + k]
        half = 0.5 * e
        out = diffused - half * (after - before) + half * e * (after - 2.0 * diffused + before)
        for j in range(nblk):
            o_ref[j, k] = out[:, j * width : (j + 1) * width]


def halo_pairs(rows, halves, fields, step):
    pairs = []
    for r in range(rows):
        for f in range(fields):
            for h in range(halves):
                nh, nr = h + step, r
                if nh == halves:
                    nh, nr = 0, r + 1
                elif nh < 0:
                    nh, nr = halves - 1, r - 1
                if 0 <= nr < rows:
                    pairs.append(((f * halves + h) * rows + r, (f * halves + nh) * rows + nr))
    return pairs


def one_round(block, offset, shear_shift, remap_fraction, diffusivity):
    nf, nrow, nz, width = block.shape
    loop = lax.axis_size("az")
    parts = loop // nf
    rows = nrow // parts
    x = block.reshape(nf * parts, rows, nz, width)
    y = lax.all_to_all(x, "az", 0, 0, tiled=True)
    length = loop * width
    smem = pl.BlockSpec(memory_space=pltpu.SMEM)
    vmem = pl.BlockSpec(memory_space=pltpu.VMEM)
    shifted, last, first, low, high = pl.pallas_call(
        functools.partial(shift_kernel, parts),
        out_shape=(
            jax.ShapeDtypeStruct((rows, nz, length), y.dtype),
            jax.ShapeDtypeStruct((1, nz, length), y.dtype),
            jax.ShapeDtypeStruct((1, nz, length), y.dtype),
            jax.ShapeDtypeStruct((rows, length), y.dtype),
            jax.ShapeDtypeStruct((rows, length), y.dtype),
        ),
        in_specs=[smem, vmem],
        out_specs=(vmem,) * 5,
    )(shear_shift, y)

    nrad = lax.axis_size("rad")
    nvert = lax.axis_size("vert")
    both = ("az", "rad")
    prev_row = lax.ppermute(last, both, halo_pairs(nrad, parts, nf, 1))
    next_row = lax.ppermute(first, both, halo_pairs(nrad, parts, nf, -1))
    up = [(i, i + 1) for i in range(nvert - 1)]
    down = [(i + 1, i) for i in range(nvert - 1)]
    below = lax.ppermute(high, "vert", up)
    above = lax.ppermute(low, "vert", down)

    blocks = pl.pallas_call(
        functools.partial(diffuse_kernel, parts, offset),
        out_shape=jax.ShapeDtypeStruct((loop, rows, nz, width), y.dtype),
        in_specs=[smem, smem] + [vmem] * 5,
        out_specs=vmem,
    )(diffusivity, remap_fraction, shifted, prev_row, next_row, below, above)
    back = lax.all_to_all(blocks, "az", 0, 0, tiled=True)
    return back.reshape(nf, nrow, nz, width)


def per_device(fields, shear_shift, remap_fraction, diffusivity):
    nf = fields.shape[0]
    step = nf // ROUNDS
    outs = [
        one_round(fields[i : i + step], i, shear_shift, remap_fraction, diffusivity)
        for i in range(0, nf, step)
    ]
    return outs[0] if len(outs) == 1 else jnp.concatenate(outs, axis=0)


def solution(mesh):
    in_specs = (P(None, "rad", "vert", "az"), P("rad"), P("rad"), P())
    out_specs = P(None, "rad", "vert", "az")
    return jax.shard_map(
        per_device, mesh=mesh, in_specs=in_specs, out_specs=out_specs, check_vma=False
    )
```

```python
import functools

import jax
import jax.numpy as jnp
from jax import lax
from jax.experimental import pallas as pl
from jax.experimental.pallas import tpu as pltpu
from jax.sharding import PartitionSpec as P


ROUNDS = 1


def shift_kernel(parts, amount_ref, x_ref, o_ref, intra_ref, cross_ref, low_ref, high_ref):
    nblk, rows, nz, width = x_ref.shape
    lane = lax.broadcasted_iota(jnp.int32, (nz, width), 1)
    h = lax.axis_index("az") % parts
    base = h * rows
    for k in range(rows):
        s = amount_ref[base + k]
        b = s // width
        rem = s % width
        late = lane >= width - rem
        for j in range(nblk):
            near = x_ref[(j - b + nblk) % nblk, k]
            far = x_ref[(j - b - 1 + 2 * nblk) % nblk, k]
            v = pltpu.roll(jnp.where(late, far, near), rem, 1)
            cols = slice(j * width, (j + 1) * width)
            o_ref[k, :, cols] = v
            low_ref[k : k + 1, cols] = v[0:1]
            high_ref[k : k + 1, cols] = v[nz - 1 : nz]
            if k == 0:

                @pl.when(h == 1)
                def _():
                    intra_ref[0, :, cols] = v

                @pl.when(h == 0)
                def _():
                    cross_ref[0, :, cols] = v

            if k == rows - 1:

                @pl.when(h == 0)
                def _():
                    intra_ref[0, :, cols] = v

                @pl.when(h == 1)
                def _():
                    cross_ref[0, :, cols] = v


def diffuse_kernel(parts, offset, c_ref, e_ref, s_ref, intra_ref, cross_ref, below_ref, above_ref, o_ref):
    nblk, rows, nz, width = o_ref.shape
    length = s_ref.shape[2]
    sub = lax.broadcasted_iota(jnp.int32, (nz, length), 0)
    me = lax.axis_index("az")
    h = me % parts
    base = h * rows
    c = c_ref[me // parts + offset]
    top = h == 0
    for k in range(rows):
        shifted = s_ref[k]
        r_plus = s_ref[k + 1] if k < rows - 1 else jnp.where(top, intra_ref[0], cross_ref[0])
        r_minus = s_ref[k - 1] if k > 0 else jnp.where(top, cross_ref[0], intra_ref[0])
        z_plus = jnp.where(sub == nz - 1, above_ref[k : k + 1, :], pltpu.roll(shifted, nz - 1, 0))
        z_minus = jnp.where(sub == 0, below_ref[k : k + 1, :], pltpu.roll(shifted, 1, 0))
        laplace = r_plus + r_minus + z_plus + z_minus - 4.0 * shifted
        diffused = shifted + c * laplace
        after = pltpu.roll(diffused, length - 1, 1)
        before = pltpu.roll(diffused, 1, 1)
        e = e_ref[base + k]
        half = 0.5 * e
        out = diffused - half * (after - before) + half * e * (after - 2.0 * diffused + before)
        for j in range(nblk):
            o_ref[j, k] = out[:, j * width : (j + 1) * width]


def cross_pairs(nrad, loop):
    pairs = []
    for a in range(loop):
        for r in range(nrad):
            if a % 2 == 1 and r + 1 < nrad:
                pairs.append((a * nrad + r, (a - 1) * nrad + r + 1))
            if a % 2 == 0 and r > 0:
                pairs.append((a * nrad + r, (a + 1) * nrad + r - 1))
    return pairs


def one_round(block, offset, shear_shift, remap_fraction, diffusivity):
    nf, nrow, nz, width = block.shape
    loop = lax.axis_size("az")
    parts = loop // nf
    assert parts == 2
    rows = nrow // parts
    x = block.reshape(nf * parts, rows, nz, width)
    y = lax.all_to_all(x, "az", 0, 0, tiled=True)
    length = loop * width
    smem = pl.BlockSpec(memory_space=pltpu.SMEM)
    vmem = pl.BlockSpec(memory_space=pltpu.VMEM)
    shifted, intra, cross, low, high = pl.pallas_call(
        functools.partial(shift_kernel, parts),
        out_shape=(
            jax.ShapeDtypeStruct((rows, nz, length), y.dtype),
            jax.ShapeDtypeStruct((1, nz, length), y.dtype),
            jax.ShapeDtypeStruct((1, nz, length), y.dtype),
            jax.ShapeDtypeStruct((rows, length), y.dtype),
            jax.ShapeDtypeStruct((rows, length), y.dtype),
        ),
        in_specs=[smem, vmem],
        out_specs=(vmem,) * 5,
    )(shear_shift, y)

    nrad = lax.axis_size("rad")
    nvert = lax.axis_size("vert")
    both = ("az", "rad")
    up = [(i, i + 1) for i in range(nvert - 1)]
    down = [(i + 1, i) for i in range(nvert - 1)]
    below = lax.ppermute(high, "vert", up)
    above = lax.ppermute(low, "vert", down)
    cross_in = lax.ppermute(cross, both, cross_pairs(nrad, loop))
    intra_in = lax.ppermute(intra, "az", [(i, i ^ 1) for i in range(loop)])

    blocks = pl.pallas_call(
        functools.partial(diffuse_kernel, parts, offset),
        out_shape=jax.ShapeDtypeStruct((loop, rows, nz, width), y.dtype),
        in_specs=[smem, smem] + [vmem] * 5,
        out_specs=vmem,
    )(diffusivity, remap_fraction, shifted, intra_in, cross_in, below, above)
    back = lax.all_to_all(blocks, "az", 0, 0, tiled=True)
    return back.reshape(nf, nrow, nz, width)


def per_device(fields, shear_shift, remap_fraction, diffusivity):
    nf = fields.shape[0]
    step = nf // ROUNDS
    outs = [
        one_round(fields[i : i + step], i, shear_shift, remap_fraction, diffusivity)
        for i in range(0, nf, step)
    ]
    return outs[0] if len(outs) == 1 else jnp.concatenate(outs, axis=0)


def solution(mesh):
    in_specs = (P(None, "rad", "vert", "az"), P("rad"), P("rad"), P())
    out_specs = P(None, "rad", "vert", "az")
    return jax.shard_map(
        per_device, mesh=mesh, in_specs=in_specs, out_specs=out_specs, check_vma=False
    )
```

```python
import functools

import jax
import jax.numpy as jnp
from jax import lax
from jax.experimental import pallas as pl
from jax.experimental.pallas import tpu as pltpu
from jax.sharding import PartitionSpec as P


ROUNDS = 1


def shift_kernel(parts, amount_ref, x_ref, o_ref, intra_ref, cross_ref, low_ref, high_ref, first_buf):
    nblk, rows, nz, width = x_ref.shape
    lane = lax.broadcasted_iota(jnp.int32, (nz, width), 1)
    h = lax.axis_index("az") % parts
    top = h == 0
    base = h * rows
    for k in range(rows):
        s = amount_ref[base + k]
        b = s // width
        rem = s % width
        late = lane >= width - rem
        for j in range(nblk):
            near = x_ref[(j - b + nblk) % nblk, k]
            far = x_ref[(j - b - 1 + 2 * nblk) % nblk, k]
            v = pltpu.roll(jnp.where(late, far, near), rem, 1)
            cols = slice(j * width, (j + 1) * width)
            o_ref[k, :, cols] = v
            low_ref[k : k + 1, cols] = v[0:1]
            high_ref[k : k + 1, cols] = v[nz - 1 : nz]
            if k == 0:
                first_buf[:, cols] = v
            if k == rows - 1:
                first = first_buf[:, cols]
                intra_ref[0, :, cols] = jnp.where(top, v, first)
                cross_ref[0, :, cols] = jnp.where(top, first, v)


def diffuse_kernel(parts, offset, c_ref, e_ref, s_ref, intra_ref, cross_ref, below_ref, above_ref, o_ref):
    nblk, rows, nz, width = o_ref.shape
    length = s_ref.shape[2]
    sub = lax.broadcasted_iota(jnp.int32, (nz, length), 0)
    me = lax.axis_index("az")
    h = me % parts
    base = h * rows
    c = c_ref[me // parts + offset]
    top = h == 0
    for k in range(rows):
        shifted = s_ref[k]
        r_plus = s_ref[k + 1] if k < rows - 1 else jnp.where(top, intra_ref[0], cross_ref[0])
        r_minus = s_ref[k - 1] if k > 0 else jnp.where(top, cross_ref[0], intra_ref[0])
        z_plus = jnp.where(sub == nz - 1, above_ref[k : k + 1, :], pltpu.roll(shifted, nz - 1, 0))
        z_minus = jnp.where(sub == 0, below_ref[k : k + 1, :], pltpu.roll(shifted, 1, 0))
        laplace = r_plus + r_minus + z_plus + z_minus - 4.0 * shifted
        diffused = shifted + c * laplace
        after = pltpu.roll(diffused, length - 1, 1)
        before = pltpu.roll(diffused, 1, 1)
        e = e_ref[base + k]
        half = 0.5 * e
        out = diffused - half * (after - before) + half * e * (after - 2.0 * diffused + before)
        for j in range(nblk):
            o_ref[j, k] = out[:, j * width : (j + 1) * width]


def cross_pairs(nrad, loop):
    pairs = []
    for a in range(loop):
        for r in range(nrad):
            if a % 2 == 1 and r + 1 < nrad:
                pairs.append((a * nrad + r, (a - 1) * nrad + r + 1))
            if a % 2 == 0 and r > 0:
                pairs.append((a * nrad + r, (a + 1) * nrad + r - 1))
    return pairs


def one_round(block, offset, shear_shift, remap_fraction, diffusivity):
    nf, nrow, nz, width = block.shape
    loop = lax.axis_size("az")
    parts = loop // nf
    assert parts == 2
    rows = nrow // parts
    x = block.reshape(nf * parts, rows, nz, width)
    y = lax.all_to_all(x, "az", 0, 0, tiled=True)
    length = loop * width
    smem = pl.BlockSpec(memory_space=pltpu.SMEM)
    vmem = pl.BlockSpec(memory_space=pltpu.VMEM)
    shifted, intra, cross, low, high = pl.pallas_call(
        functools.partial(shift_kernel, parts),
        out_shape=(
            jax.ShapeDtypeStruct((rows, nz, length), y.dtype),
            jax.ShapeDtypeStruct((1, nz, length), y.dtype),
            jax.ShapeDtypeStruct((1, nz, length), y.dtype),
            jax.ShapeDtypeStruct((rows, length), y.dtype),
            jax.ShapeDtypeStruct((rows, length), y.dtype),
        ),
        in_specs=[smem, vmem],
        out_specs=(vmem,) * 5,
        scratch_shapes=[pltpu.VMEM((nz, length), y.dtype)],
    )(shear_shift, y)

    nrad = lax.axis_size("rad")
    nvert = lax.axis_size("vert")
    both = ("az", "rad")
    up = [(i, i + 1) for i in range(nvert - 1)]
    down = [(i + 1, i) for i in range(nvert - 1)]
    below = lax.ppermute(high, "vert", up)
    above = lax.ppermute(low, "vert", down)
    cross_in = lax.ppermute(cross, both, cross_pairs(nrad, loop))
    intra_in = lax.ppermute(intra, "az", [(i, i ^ 1) for i in range(loop)])

    blocks = pl.pallas_call(
        functools.partial(diffuse_kernel, parts, offset),
        out_shape=jax.ShapeDtypeStruct((loop, rows, nz, width), y.dtype),
        in_specs=[smem, smem] + [vmem] * 5,
        out_specs=vmem,
    )(diffusivity, remap_fraction, shifted, intra_in, cross_in, below, above)
    back = lax.all_to_all(blocks, "az", 0, 0, tiled=True)
    return back.reshape(nf, nrow, nz, width)


def per_device(fields, shear_shift, remap_fraction, diffusivity):
    nf = fields.shape[0]
    step = nf // ROUNDS
    outs = [
        one_round(fields[i : i + step], i, shear_shift, remap_fraction, diffusivity)
        for i in range(0, nf, step)
    ]
    return outs[0] if len(outs) == 1 else jnp.concatenate(outs, axis=0)


def solution(mesh):
    in_specs = (P(None, "rad", "vert", "az"), P("rad"), P("rad"), P())
    out_specs = P(None, "rad", "vert", "az")
    return jax.shard_map(
        per_device, mesh=mesh, in_specs=in_specs, out_specs=out_specs, check_vma=False
    )
```

```python
import functools

import jax
import jax.numpy as jnp
from jax import lax
from jax.experimental import pallas as pl
from jax.experimental.pallas import tpu as pltpu
from jax.sharding import PartitionSpec as P


ROUNDS = 1
LP = pltpu.CompilerParams()


def shift_kernel(parts, amount_ref, x_ref, o_ref, last_ref, first_ref, low_ref, high_ref):
    nblk, rows, nz, width = x_ref.shape
    lane = lax.broadcasted_iota(jnp.int32, (nz, width), 1)
    base = lax.axis_index("az") % parts * rows
    wrap = nblk - 1
    for k in range(rows):
        s = amount_ref[base + k]
        b = s // width
        rem = s % width
        late = lane >= width - rem
        for j in range(nblk):
            near = x_ref[(j - b) & wrap, k]
            far = x_ref[(j - b - 1) & wrap, k]
            v = pltpu.roll(jnp.where(late, far, near), rem, 1)
            cols = slice(j * width, (j + 1) * width)
            o_ref[k, :, cols] = v
            low_ref[k : k + 1, cols] = v[0:1]
            high_ref[k : k + 1, cols] = v[nz - 1 : nz]
            if k == 0:
                first_ref[0, :, cols] = v
            if k == rows - 1:
                last_ref[0, :, cols] = v


def diffuse_kernel(parts, offset, c_ref, e_ref, s_ref, prev_ref, next_ref, below_ref, above_ref, o_ref):
    nblk, rows, nz, width = o_ref.shape
    length = s_ref.shape[2]
    sub = lax.broadcasted_iota(jnp.int32, (nz, length), 0)
    me = lax.axis_index("az")
    base = me % parts * rows
    c = c_ref[me // parts + offset]
    for k in range(rows):
        shifted = s_ref[k]
        r_plus = s_ref[k + 1] if k < rows - 1 else next_ref[0]
        r_minus = s_ref[k - 1] if k > 0 else prev_ref[0]
        z_plus = jnp.where(sub == nz - 1, above_ref[k : k + 1, :], pltpu.roll(shifted, nz - 1, 0))
        z_minus = jnp.where(sub == 0, below_ref[k : k + 1, :], pltpu.roll(shifted, 1, 0))
        laplace = r_plus + r_minus + z_plus + z_minus - 4.0 * shifted
        diffused = shifted + c * laplace
        after = pltpu.roll(diffused, length - 1, 1)
        before = pltpu.roll(diffused, 1, 1)
        e = e_ref[base + k]
        half = 0.5 * e
        out = diffused - half * (after - before) + half * e * (after - 2.0 * diffused + before)
        for j in range(nblk):
            o_ref[j, k] = out[:, j * width : (j + 1) * width]


def halo_pairs(rows, halves, fields, step):
    pairs = []
    for r in range(rows):
        for f in range(fields):
            for h in range(halves):
                nh, nr = h + step, r
                if nh == halves:
                    nh, nr = 0, r + 1
                elif nh < 0:
                    nh, nr = halves - 1, r - 1
                if 0 <= nr < rows:
                    pairs.append(((f * halves + h) * rows + r, (f * halves + nh) * rows + nr))
    return pairs


def one_round(block, offset, shear_shift, remap_fraction, diffusivity):
    nf, nrow, nz, width = block.shape
    loop = lax.axis_size("az")
    parts = loop // nf
    assert loop & (loop - 1) == 0
    rows = nrow // parts
    x = block.reshape(nf * parts, rows, nz, width)
    y = lax.all_to_all(x, "az", 0, 0, tiled=True)
    length = loop * width
    smem = pl.BlockSpec(memory_space=pltpu.SMEM)
    vmem = pl.BlockSpec(memory_space=pltpu.VMEM)
    shifted, last, first, low, high = pl.pallas_call(
        functools.partial(shift_kernel, parts),
        out_shape=(
            jax.ShapeDtypeStruct((rows, nz, length), y.dtype),
            jax.ShapeDtypeStruct((1, nz, length), y.dtype),
            jax.ShapeDtypeStruct((1, nz, length), y.dtype),
            jax.ShapeDtypeStruct((rows, length), y.dtype),
            jax.ShapeDtypeStruct((rows, length), y.dtype),
        ),
        in_specs=[smem, vmem],
        out_specs=(vmem,) * 5,
        compiler_params=LP,
    )(shear_shift, y)

    nrad = lax.axis_size("rad")
    nvert = lax.axis_size("vert")
    both = ("az", "rad")
    up = [(i, i + 1) for i in range(nvert - 1)]
    down = [(i + 1, i) for i in range(nvert - 1)]
    below = lax.ppermute(high, "vert", up)
    above = lax.ppermute(low, "vert", down)
    prev_row = lax.ppermute(last, both, halo_pairs(nrad, parts, nf, 1))
    next_row = lax.ppermute(first, both, halo_pairs(nrad, parts, nf, -1))

    blocks = pl.pallas_call(
        functools.partial(diffuse_kernel, parts, offset),
        out_shape=jax.ShapeDtypeStruct((loop, rows, nz, width), y.dtype),
        in_specs=[smem, smem] + [vmem] * 5,
        out_specs=vmem,
        compiler_params=LP,
    )(diffusivity, remap_fraction, shifted, prev_row, next_row, below, above)
    back = lax.all_to_all(blocks, "az", 0, 0, tiled=True)
    return back.reshape(nf, nrow, nz, width)


def per_device(fields, shear_shift, remap_fraction, diffusivity):
    nf = fields.shape[0]
    step = nf // ROUNDS
    outs = [
        one_round(fields[i : i + step], i, shear_shift, remap_fraction, diffusivity)
        for i in range(0, nf, step)
    ]
    return outs[0] if len(outs) == 1 else jnp.concatenate(outs, axis=0)


def solution(mesh):
    in_specs = (P(None, "rad", "vert", "az"), P("rad"), P("rad"), P())
    out_specs = P(None, "rad", "vert", "az")
    return jax.shard_map(
        per_device, mesh=mesh, in_specs=in_specs, out_specs=out_specs, check_vma=False
    )
```

```python
import functools

import jax
import jax.numpy as jnp
from jax import lax
from jax.experimental import pallas as pl
from jax.experimental.pallas import tpu as pltpu
from jax.sharding import PartitionSpec as P


ROUNDS = 1


def shift_kernel(parts, amount_ref, x_ref, o_ref, last_ref, first_ref, low_ref, high_ref):
    nblk, rows, nz, width = x_ref.shape
    lane = lax.broadcasted_iota(jnp.int32, (nz, width), 1)
    base = lax.axis_index("az") % parts * rows
    wrap = nblk - 1
    for k in range(rows):
        s = amount_ref[base + k]
        b = s // width
        rem = s % width
        late = lane >= width - rem
        for j in range(nblk):
            near = x_ref[(j - b) & wrap, k]
            far = x_ref[(j - b - 1) & wrap, k]
            v = pltpu.roll(jnp.where(late, far, near), rem, 1)
            cols = slice(j * width, (j + 1) * width)
            o_ref[k, :, cols] = v
            if k == 0:
                first_ref[0, :, cols] = v
            if k == rows - 1:
                last_ref[0, :, cols] = v
    low_ref[...] = o_ref[:, 0, :]
    high_ref[...] = o_ref[:, nz - 1, :]


def diffuse_kernel(parts, offset, c_ref, e_ref, s_ref, prev_ref, next_ref, below_ref, above_ref, o_ref):
    nblk, rows, nz, width = o_ref.shape
    length = s_ref.shape[2]
    sub = lax.broadcasted_iota(jnp.int32, (nz, length), 0)
    me = lax.axis_index("az")
    base = me % parts * rows
    c = c_ref[me // parts + offset]
    for k in range(rows):
        shifted = s_ref[k]
        r_plus = s_ref[k + 1] if k < rows - 1 else next_ref[0]
        r_minus = s_ref[k - 1] if k > 0 else prev_ref[0]
        z_plus = jnp.where(sub == nz - 1, above_ref[k : k + 1, :], pltpu.roll(shifted, nz - 1, 0))
        z_minus = jnp.where(sub == 0, below_ref[k : k + 1, :], pltpu.roll(shifted, 1, 0))
        laplace = r_plus + r_minus + z_plus + z_minus - 4.0 * shifted
        diffused = shifted + c * laplace
        after = pltpu.roll(diffused, length - 1, 1)
        before = pltpu.roll(diffused, 1, 1)
        e = e_ref[base + k]
        half = 0.5 * e
        out = diffused - half * (after - before) + half * e * (after - 2.0 * diffused + before)
        for j in range(nblk):
            o_ref[j, k] = out[:, j * width : (j + 1) * width]


def halo_pairs(rows, halves, fields, step):
    pairs = []
    for r in range(rows):
        for f in range(fields):
            for h in range(halves):
                nh, nr = h + step, r
                if nh == halves:
                    nh, nr = 0, r + 1
                elif nh < 0:
                    nh, nr = halves - 1, r - 1
                if 0 <= nr < rows:
                    pairs.append(((f * halves + h) * rows + r, (f * halves + nh) * rows + nr))
    return pairs


def one_round(block, offset, shear_shift, remap_fraction, diffusivity):
    nf, nrow, nz, width = block.shape
    loop = lax.axis_size("az")
    parts = loop // nf
    assert loop & (loop - 1) == 0
    rows = nrow // parts
    x = block.reshape(nf * parts, rows, nz, width)
    y = lax.all_to_all(x, "az", 0, 0, tiled=True)
    length = loop * width
    smem = pl.BlockSpec(memory_space=pltpu.SMEM)
    vmem = pl.BlockSpec(memory_space=pltpu.VMEM)
    shifted, last, first, low, high = pl.pallas_call(
        functools.partial(shift_kernel, parts),
        out_shape=(
            jax.ShapeDtypeStruct((rows, nz, length), y.dtype),
            jax.ShapeDtypeStruct((1, nz, length), y.dtype),
            jax.ShapeDtypeStruct((1, nz, length), y.dtype),
            jax.ShapeDtypeStruct((rows, length), y.dtype),
            jax.ShapeDtypeStruct((rows, length), y.dtype),
        ),
        in_specs=[smem, vmem],
        out_specs=(vmem,) * 5,
    )(shear_shift, y)

    nrad = lax.axis_size("rad")
    nvert = lax.axis_size("vert")
    both = ("az", "rad")
    up = [(i, i + 1) for i in range(nvert - 1)]
    down = [(i + 1, i) for i in range(nvert - 1)]
    below = lax.ppermute(high, "vert", up)
    above = lax.ppermute(low, "vert", down)
    prev_row = lax.ppermute(last, both, halo_pairs(nrad, parts, nf, 1))
    next_row = lax.ppermute(first, both, halo_pairs(nrad, parts, nf, -1))

    blocks = pl.pallas_call(
        functools.partial(diffuse_kernel, parts, offset),
        out_shape=jax.ShapeDtypeStruct((loop, rows, nz, width), y.dtype),
        in_specs=[smem, smem] + [vmem] * 5,
        out_specs=vmem,
    )(diffusivity, remap_fraction, shifted, prev_row, next_row, below, above)
    back = lax.all_to_all(blocks, "az", 0, 0, tiled=True)
    return back.reshape(nf, nrow, nz, width)


def per_device(fields, shear_shift, remap_fraction, diffusivity):
    nf = fields.shape[0]
    step = nf // ROUNDS
    outs = [
        one_round(fields[i : i + step], i, shear_shift, remap_fraction, diffusivity)
        for i in range(0, nf, step)
    ]
    return outs[0] if len(outs) == 1 else jnp.concatenate(outs, axis=0)


def solution(mesh):
    in_specs = (P(None, "rad", "vert", "az"), P("rad"), P("rad"), P())
    out_specs = P(None, "rad", "vert", "az")
    return jax.shard_map(
        per_device, mesh=mesh, in_specs=in_specs, out_specs=out_specs, check_vma=False
    )
```

```python
import functools

import jax
import jax.numpy as jnp
from jax import lax
from jax.experimental import pallas as pl
from jax.experimental.pallas import tpu as pltpu
from jax.sharding import PartitionSpec as P


ROUNDS = 1


def shift_kernel(parts, amount_ref, x_ref, o_ref, last_ref, first_ref, low_ref, high_ref):
    nblk, rows, nz, width = x_ref.shape
    lane = lax.broadcasted_iota(jnp.int32, (nz, width), 1)
    base = lax.axis_index("az") % parts * rows
    wrap = nblk - 1
    for k in range(rows):
        s = amount_ref[base + k]
        b = s // width
        rem = s % width
        late = lane >= width - rem
        for j in range(nblk):
            near = x_ref[(j - b) & wrap, k]
            far = x_ref[(j - b - 1) & wrap, k]
            v = pltpu.roll(jnp.where(late, far, near), rem, 1)
            cols = slice(j * width, (j + 1) * width)
            o_ref[k, :, cols] = v
            if k == 0:
                first_ref[0, :, cols] = v
            if k == rows - 1:
                last_ref[0, :, cols] = v
    low_ref[...] = o_ref[:, 0, :]
    high_ref[...] = o_ref[:, nz - 1, :]


def diffuse_kernel(parts, offset, c_ref, e_ref, s_ref, prev_ref, next_ref, below_ref, above_ref, o_ref):
    nblk, rows, nz, width = o_ref.shape
    length = s_ref.shape[2]
    sub = lax.broadcasted_iota(jnp.int32, (nz, length), 0)
    me = lax.axis_index("az")
    base = me % parts * rows
    c = c_ref[me // parts + offset]
    r_minus = prev_ref[0]
    shifted = s_ref[0]
    for k in range(rows):
        r_plus = s_ref[k + 1] if k < rows - 1 else next_ref[0]
        z_plus = jnp.where(sub == nz - 1, above_ref[k : k + 1, :], pltpu.roll(shifted, nz - 1, 0))
        z_minus = jnp.where(sub == 0, below_ref[k : k + 1, :], pltpu.roll(shifted, 1, 0))
        laplace = r_plus + r_minus + z_plus + z_minus - 4.0 * shifted
        diffused = shifted + c * laplace
        after = pltpu.roll(diffused, length - 1, 1)
        before = pltpu.roll(diffused, 1, 1)
        e = e_ref[base + k]
        half = 0.5 * e
        out = diffused - half * (after - before) + half * e * (after - 2.0 * diffused + before)
        for j in range(nblk):
            o_ref[j, k] = out[:, j * width : (j + 1) * width]
        r_minus, shifted = shifted, r_plus


def halo_pairs(rows, halves, fields, step):
    pairs = []
    for r in range(rows):
        for f in range(fields):
            for h in range(halves):
                nh, nr = h + step, r
                if nh == halves:
                    nh, nr = 0, r + 1
                elif nh < 0:
                    nh, nr = halves - 1, r - 1
                if 0 <= nr < rows:
                    pairs.append(((f * halves + h) * rows + r, (f * halves + nh) * rows + nr))
    return pairs


def one_round(block, offset, shear_shift, remap_fraction, diffusivity):
    nf, nrow, nz, width = block.shape
    loop = lax.axis_size("az")
    parts = loop // nf
    assert loop & (loop - 1) == 0
    rows = nrow // parts
    x = block.reshape(nf * parts, rows, nz, width)
    y = lax.all_to_all(x, "az", 0, 0, tiled=True)
    length = loop * width
    smem = pl.BlockSpec(memory_space=pltpu.SMEM)
    vmem = pl.BlockSpec(memory_space=pltpu.VMEM)
    shifted, last, first, low, high = pl.pallas_call(
        functools.partial(shift_kernel, parts),
        out_shape=(
            jax.ShapeDtypeStruct((rows, nz, length), y.dtype),
            jax.ShapeDtypeStruct((1, nz, length), y.dtype),
            jax.ShapeDtypeStruct((1, nz, length), y.dtype),
            jax.ShapeDtypeStruct((rows, length), y.dtype),
            jax.ShapeDtypeStruct((rows, length), y.dtype),
        ),
        in_specs=[smem, vmem],
        out_specs=(vmem,) * 5,
    )(shear_shift, y)

    nrad = lax.axis_size("rad")
    nvert = lax.axis_size("vert")
    both = ("az", "rad")
    up = [(i, i + 1) for i in range(nvert - 1)]
    down = [(i + 1, i) for i in range(nvert - 1)]
    below = lax.ppermute(high, "vert", up)
    above = lax.ppermute(low, "vert", down)
    prev_row = lax.ppermute(last, both, halo_pairs(nrad, parts, nf, 1))
    next_row = lax.ppermute(first, both, halo_pairs(nrad, parts, nf, -1))

    blocks = pl.pallas_call(
        functools.partial(diffuse_kernel, parts, offset),
        out_shape=jax.ShapeDtypeStruct((loop, rows, nz, width), y.dtype),
        in_specs=[smem, smem] + [vmem] * 5,
        out_specs=vmem,
    )(diffusivity, remap_fraction, shifted, prev_row, next_row, below, above)
    back = lax.all_to_all(blocks, "az", 0, 0, tiled=True)
    return back.reshape(nf, nrow, nz, width)


def per_device(fields, shear_shift, remap_fraction, diffusivity):
    nf = fields.shape[0]
    step = nf // ROUNDS
    outs = [
        one_round(fields[i : i + step], i, shear_shift, remap_fraction, diffusivity)
        for i in range(0, nf, step)
    ]
    return outs[0] if len(outs) == 1 else jnp.concatenate(outs, axis=0)


def solution(mesh):
    in_specs = (P(None, "rad", "vert", "az"), P("rad"), P("rad"), P())
    out_specs = P(None, "rad", "vert", "az")
    return jax.shard_map(
        per_device, mesh=mesh, in_specs=in_specs, out_specs=out_specs, check_vma=False
    )
```

```python
import functools

import jax
import jax.numpy as jnp
from jax import lax
from jax.experimental import pallas as pl
from jax.experimental.pallas import tpu as pltpu
from jax.sharding import PartitionSpec as P


ROUNDS = 1


def shift_kernel(parts, amount_ref, x_ref, o_ref, last_ref, first_ref, low_ref, high_ref):
    nblk, rows, nz, width = x_ref.shape
    lane = lax.broadcasted_iota(jnp.int32, (nz, width), 1)
    base = lax.axis_index("az") % parts * rows
    wrap = nblk - 1
    for k in range(rows):
        s = amount_ref[base + k]
        b = s >> (width.bit_length() - 1)
        rem = s & (width - 1)
        late = lane >= width - rem
        for j in range(nblk):
            near = x_ref[(j - b) & wrap, k]
            far = x_ref[(j - b - 1) & wrap, k]
            v = pltpu.roll(jnp.where(late, far, near), rem, 1)
            cols = slice(j * width, (j + 1) * width)
            o_ref[k, :, cols] = v
            if k == 0:
                first_ref[0, :, cols] = v
            if k == rows - 1:
                last_ref[0, :, cols] = v
    low_ref[...] = o_ref[:, 0, :]
    high_ref[...] = o_ref[:, nz - 1, :]


def diffuse_kernel(parts, offset, c_ref, e_ref, s_ref, prev_ref, next_ref, below_ref, above_ref, o_ref):
    nblk, rows, nz, width = o_ref.shape
    length = s_ref.shape[2]
    sub = lax.broadcasted_iota(jnp.int32, (nz, length), 0)
    me = lax.axis_index("az")
    base = me % parts * rows
    c = c_ref[me // parts + offset]
    r_minus = prev_ref[0]
    shifted = s_ref[0]
    for k in range(rows):
        r_plus = s_ref[k + 1] if k < rows - 1 else next_ref[0]
        z_plus = jnp.where(sub == nz - 1, above_ref[k : k + 1, :], pltpu.roll(shifted, nz - 1, 0))
        z_minus = jnp.where(sub == 0, below_ref[k : k + 1, :], pltpu.roll(shifted, 1, 0))
        laplace = r_plus + r_minus + z_plus + z_minus - 4.0 * shifted
        diffused = shifted + c * laplace
        after = pltpu.roll(diffused, length - 1, 1)
        before = pltpu.roll(diffused, 1, 1)
        e = e_ref[base + k]
        half = 0.5 * e
        out = diffused - half * (after - before) + half * e * (after - 2.0 * diffused + before)
        for j in range(nblk):
            o_ref[j, k] = out[:, j * width : (j + 1) * width]
        r_minus, shifted = shifted, r_plus


def halo_pairs(rows, halves, fields, step):
    pairs = []
    for r in range(rows):
        for f in range(fields):
            for h in range(halves):
                nh, nr = h + step, r
                if nh == halves:
                    nh, nr = 0, r + 1
                elif nh < 0:
                    nh, nr = halves - 1, r - 1
                if 0 <= nr < rows:
                    pairs.append(((f * halves + h) * rows + r, (f * halves + nh) * rows + nr))
    return pairs


def one_round(block, offset, shear_shift, remap_fraction, diffusivity):
    nf, nrow, nz, width = block.shape
    loop = lax.axis_size("az")
    parts = loop // nf
    assert loop & (loop - 1) == 0 and width & (width - 1) == 0
    rows = nrow // parts
    x = block.reshape(nf * parts, rows, nz, width)
    y = lax.all_to_all(x, "az", 0, 0, tiled=True)
    length = loop * width
    smem = pl.BlockSpec(memory_space=pltpu.SMEM)
    vmem = pl.BlockSpec(memory_space=pltpu.VMEM)
    shifted, last, first, low, high = pl.pallas_call(
        functools.partial(shift_kernel, parts),
        out_shape=(
            jax.ShapeDtypeStruct((rows, nz, length), y.dtype),
            jax.ShapeDtypeStruct((1, nz, length), y.dtype),
            jax.ShapeDtypeStruct((1, nz, length), y.dtype),
            jax.ShapeDtypeStruct((rows, length), y.dtype),
            jax.ShapeDtypeStruct((rows, length), y.dtype),
        ),
        in_specs=[smem, vmem],
        out_specs=(vmem,) * 5,
    )(shear_shift, y)

    nrad = lax.axis_size("rad")
    nvert = lax.axis_size("vert")
    both = ("az", "rad")
    up = [(i, i + 1) for i in range(nvert - 1)]
    down = [(i + 1, i) for i in range(nvert - 1)]
    below = lax.ppermute(high, "vert", up)
    above = lax.ppermute(low, "vert", down)
    prev_row = lax.ppermute(last, both, halo_pairs(nrad, parts, nf, 1))
    next_row = lax.ppermute(first, both, halo_pairs(nrad, parts, nf, -1))

    blocks = pl.pallas_call(
        functools.partial(diffuse_kernel, parts, offset),
        out_shape=jax.ShapeDtypeStruct((loop, rows, nz, width), y.dtype),
        in_specs=[smem, smem] + [vmem] * 5,
        out_specs=vmem,
    )(diffusivity, remap_fraction, shifted, prev_row, next_row, below, above)
    back = lax.all_to_all(blocks, "az", 0, 0, tiled=True)
    return back.reshape(nf, nrow, nz, width)


def per_device(fields, shear_shift, remap_fraction, diffusivity):
    nf = fields.shape[0]
    step = nf // ROUNDS
    outs = [
        one_round(fields[i : i + step], i, shear_shift, remap_fraction, diffusivity)
        for i in range(0, nf, step)
    ]
    return outs[0] if len(outs) == 1 else jnp.concatenate(outs, axis=0)


def solution(mesh):
    in_specs = (P(None, "rad", "vert", "az"), P("rad"), P("rad"), P())
    out_specs = P(None, "rad", "vert", "az")
    return jax.shard_map(
        per_device, mesh=mesh, in_specs=in_specs, out_specs=out_specs, check_vma=False
    )
```
